768 devices in a mesh: lat: 96 (over x, z, y_lo), lon: 8 (over y_hi, core).
Axes of the slice: x: 4, y: 8 (y_hi: 4, y_lo: 2; y = y_hi * 2 + y_lo), z: 12, core: 2. Of those that a mesh axis runs over, the one named last changes fastest.
Arguments:
- field: float32 [32, 1536, 1024], P(None, 'lat', 'lon'), may hold values from -6 to 6
- w_first: float32 [32, 32, 3, 3], replicated, may hold values from -0.375 to 0.375
- w_second: float32 [32, 32, 3, 3], replicated, may hold values from -0.375 to 0.375
- w_down: float32 [128, 32, 3, 3], replicated, may hold values from -0.375 to 0.375
- w_query: float32 [512, 128], replicated, may hold values from -0.5 to 0.5
- w_key: float32 [512, 128], replicated, may hold values from -0.5 to 0.5
- w_value: float32 [512, 128], replicated, may hold values from -0.5 to 0.5
- w_out: float32 [128, 512], replicated, may hold values from -0.25 to 0.25
- score_scale: float32 [8], replicated, may hold values from 2 to 12
- w_up: float32 [128, 256, 3, 3], replicated, may hold values from -0.125 to 0.125
- w_last: float32 [32, 160, 3, 3], replicated, may hold values from -0.15625 to 0.15625
Outputs:
- result: float32 [32, 1536, 1024], P(None, 'lat', 'lon')
The draws below stay inside these ranges and needn't reach their ends.
All inputs are finite; a program needn't handle non-finite values.
Results may differ from the reference program's by a relative error of at most 0.0003.
Values sent between devices are 32-bit elements; how exact they have to be, the bound alone decides.
No kernel may reach another device: no remote copies, remote signals or barrier semaphores. Data moves between devices by JAX's collectives and lax.ppermute only.
A program may use at most 32 MiB of HBM per device.

```python
import math
import jax
import jax.numpy as jnp
from jax import lax

CH = 32
MID = 128
WIDE = 512
HEADS = 8
LAT_DEV = 16
NLAT = 1536
NLON = 1024
N_LAT = 96


def steps_of(rng, shape, pieces, least, high):
    def one(dim, shards_of):
        draws = jax.random.uniform(jax.random.fold_in(jax.random.fold_in(rng, 6), dim), (shards_of,), jnp.float32, least / len(pieces), high / len(pieces))
        return jnp.repeat(jnp.exp(draws), shape[dim] // shards_of).reshape((-1,) + (1,) * (len(shape) - dim - 1))

    loudness = one(*pieces[0])
    for cut in pieces[1:]:
        loudness = loudness * one(*cut)
    return loudness


def bell_draw(own_key, shape, scale, most, split=(), held_as=jnp.bfloat16):
    array = scale * jax.random.normal(own_key, shape, jnp.float32)
    if split:
        array = array * steps_of(own_key, shape, split, -0.22, 0.18)
    return jnp.clip(array, -most, most).astype(held_as)


def setup_inputs(seed: int = 0) -> dict:
    seeds = jax.random.split(jax.random.key(seed), 12)
    return {
        "field": bell_draw(seeds[0], (CH, NLAT, NLON), 1.0, 6.0, ((1, 96), (2, 8)), jnp.float32),
        "w_first": bell_draw(seeds[1], (CH, CH, 3, 3), (9 * CH) ** -0.5, 0.375, (), jnp.float32),
        "w_second": bell_draw(seeds[2], (CH, CH, 3, 3), (9 * CH) ** -0.5, 0.375, (), jnp.float32),
        "w_down": bell_draw(seeds[3], (MID, CH, 3, 3), (9 * CH) ** -0.5, 0.375, (), jnp.float32),
        "w_query": bell_draw(seeds[4], (WIDE, MID), MID ** -0.5, 0.5, (), jnp.float32),
        "w_key": bell_draw(seeds[5], (WIDE, MID), MID ** -0.5, 0.5, (), jnp.float32),
        "w_value": bell_draw(seeds[6], (WIDE, MID), MID ** -0.5, 0.5, (), jnp.float32),
        "w_out": bell_draw(seeds[7], (MID, WIDE), WIDE ** -0.5, 0.25, (), jnp.float32),
        "score_scale": jnp.clip(jnp.exp(jax.random.uniform(seeds[8], (HEADS,), jnp.float32, math.log(2.0), math.log(12.0))), 2.0, 12.0),
        "w_up": bell_draw(seeds[9], (MID, 2 * MID, 3, 3), (18 * MID) ** -0.5, 0.125, (), jnp.float32),
        "w_last": bell_draw(seeds[10], (CH, MID + CH, 3, 3), (9 * (MID + CH)) ** -0.5, 0.15625, (), jnp.float32),
    }


EPSILON = 1e-06
HIGH = lax.Precision.HIGHEST

def pad_grid(values):
    rows = jnp.pad(values, ((0, 0), (1, 1), (0, 0)))
    return jnp.concatenate([rows[:, :, -1:], rows, rows[:, :, :1]], axis=2)

def convolve(extended, weight):
    output = lax.conv_general_dilated(extended[None], weight, (1, 1), 'VALID', dimension_numbers=('NCHW', 'OIHW', 'NCHW'), precision=HIGH)
    return output[0]

def pool_cells(values):
    chans, height, width = values.shape
    return values.reshape(chans, height // 4, 4, width // 4, 4).mean(axis=(2, 4))

def upsample(values):
    return jnp.repeat(jnp.repeat(values, 4, axis=1), 4, axis=2)

def attend(stacked, scales):
    query, keys, values = (stacked[0], stacked[1], stacked[2])
    query = query * lax.rsqrt(lax.optimization_barrier(jnp.mean(query * query, axis=1, keepdims=True)) + EPSILON)
    keys = keys * lax.rsqrt(lax.optimization_barrier(jnp.mean(keys * keys, axis=1, keepdims=True)) + EPSILON)
    scores = jnp.einsum('hdri,hdrj->hrij', query, keys, precision=HIGH)
    scores = scores * (scales / query.shape[1])[:, None, None, None]
    weights = jnp.exp(scores)
    weights = weights / lax.optimization_barrier(jnp.sum(weights, axis=3, keepdims=True))
    return jnp.einsum('hrij,hdrj->hdri', weights, values, precision=HIGH)

def reference(field, w_first, w_second, w_down, w_query, w_key, w_value, w_out, score_scale, w_up, w_last):
    first = jax.nn.silu(convolve(pad_grid(field), w_first))
    second = jax.nn.silu(convolve(pad_grid(first), w_second))
    coarse = jax.nn.silu(convolve(pad_grid(pool_cells(second)), w_down))
    summary = pool_cells(coarse)
    rows, spots = (summary.shape[1], summary.shape[2])
    head_dim = WIDE // HEADS
    weights_all = jnp.stack([w_query, w_key, w_value])
    projected = jnp.einsum('kwc,crp->kwrp', weights_all, summary, precision=HIGH).reshape(3, HEADS, head_dim, rows, spots)
    attended = attend(projected, score_scale).reshape(WIDE, rows, spots)
    mixed = summary + jnp.einsum('cw,wrp->crp', w_out, attended, precision=HIGH)
    joined = jnp.concatenate([upsample(mixed), coarse], axis=0)
    lifted = jax.nn.silu(convolve(pad_grid(joined), w_up))
    lifted_pad = pad_grid(lifted)
    second_pad = pad_grid(second)

    def band(index):
        start = (index * LAT_DEV).astype(jnp.int32)
        coarse_rows = lax.dynamic_slice_in_dim(lifted_pad, (start // 4).astype(jnp.int32), LAT_DEV // 4 + 2, 1)
        wide_rows = upsample(coarse_rows)[:, 3:-3, 3:-3]
        skip_rows = lax.dynamic_slice_in_dim(second_pad, start, LAT_DEV + 2, 1)
        return convolve(jnp.concatenate([wide_rows, skip_rows], axis=0), w_last)
    bands = lax.map(band, jnp.arange(N_LAT, dtype=jnp.int32))
    return jnp.transpose(bands, (1, 0, 2, 3)).reshape(CH, NLAT, NLON)
```

```python
import jax
import jax.numpy as jnp
from jax import lax
from jax.sharding import PartitionSpec as P

HEADS = 8


EPSILON = 1e-06
HIGH = lax.Precision.HIGHEST


def shifted(piece, dlat, dlon):
    n_lat, n_lon = (lax.axis_size("lat"), lax.axis_size("lon"))
    shape = piece.shape
    flat = piece.reshape(-1)
    if dlon == 0:
        pairs = [(a, a + dlat) for a in range(n_lat) if 0 <= a + dlat < n_lat]
        moved = lax.ppermute(flat, "lat", pairs)
    elif dlat == 0:
        pairs = [(b, (b + dlon) % n_lon) for b in range(n_lon)]
        moved = lax.ppermute(flat, "lon", pairs)
    else:
        pairs = [
            (a * n_lon + b, (a + dlat) * n_lon + (b + dlon) % n_lon)
            for a in range(n_lat)
            if 0 <= a + dlat < n_lat
            for b in range(n_lon)
        ]
        moved = lax.ppermute(flat, ("lat", "lon"), pairs)
    return moved.reshape(shape)


def halo(value, width):
    _, height, wide = value.shape
    lo, hi = (slice(0, width), slice(height - width, height))
    left, right = (slice(0, width), slice(wide - width, wide))
    top = shifted(value[:, hi, :], 1, 0)
    bottom = shifted(value[:, lo, :], -1, 0)
    west = shifted(value[:, :, right], 0, 1)
    east = shifted(value[:, :, left], 0, -1)
    top_west = shifted(value[:, hi, right], 1, 1)
    top_east = shifted(value[:, hi, left], 1, -1)
    bottom_west = shifted(value[:, lo, right], -1, 1)
    bottom_east = shifted(value[:, lo, left], -1, -1)
    rows = [
        jnp.concatenate([top_west, top, top_east], axis=2),
        jnp.concatenate([west, value, east], axis=2),
        jnp.concatenate([bottom_west, bottom, bottom_east], axis=2),
    ]
    return jnp.concatenate(rows, axis=1)


def inside_rows(value, width, height):
    first = lax.axis_index("lat") * height - width
    rows = first + lax.broadcasted_iota(jnp.int32, (1, value.shape[1], 1), 1)
    keep = (rows >= 0) & (rows < lax.axis_size("lat") * height)
    return jnp.where(keep, value, 0.0)


def convolve(extended, weight):
    output = lax.conv_general_dilated(
        extended[None],
        weight,
        (1, 1),
        "VALID",
        dimension_numbers=("NCHW", "OIHW", "NCHW"),
        precision=HIGH,
    )
    return output[0]


def pool_cells(values):
    chans, height, width = values.shape
    return values.reshape(chans, height // 4, 4, width // 4, 4).mean(axis=(2, 4))


def upsample(values):
    return jnp.repeat(jnp.repeat(values, 4, axis=1), 4, axis=2)


def attend(stacked, scales):
    query, keys, values = (stacked[0], stacked[1], stacked[2])
    query = query * lax.rsqrt(jnp.mean(query * query, axis=1, keepdims=True) + EPSILON)
    keys = keys * lax.rsqrt(jnp.mean(keys * keys, axis=1, keepdims=True) + EPSILON)
    scores = jnp.einsum("hdri,hdrj->hrij", query, keys, precision=HIGH)
    scores = scores * (scales / query.shape[1])[:, None, None, None]
    weights = jnp.exp(scores)
    weights = weights / jnp.sum(weights, axis=3, keepdims=True)
    return jnp.einsum("hrij,hdrj->hdri", weights, values, precision=HIGH)


def on_device(
    field, w_first, w_second, w_down, w_query, w_key, w_value, w_out, score_scale, w_up, w_last
):
    _, height, wide = field.shape
    coarse_h = height // 4
    field_ext = halo(field, 3)
    first = inside_rows(jax.nn.silu(convolve(field_ext, w_first)), 2, height)
    second = inside_rows(jax.nn.silu(convolve(first, w_second)), 1, height)
    pooled = pool_cells(second[:, 1 : 1 + height, 1 : 1 + wide])
    coarse = inside_rows(jax.nn.silu(convolve(halo(pooled, 3), w_down)), 2, coarse_h)
    summary = pool_cells(coarse[:, 2 : 2 + coarse_h, 2 : 2 + wide // 4])
    circle = lax.all_gather(summary, "lon", axis=2, tiled=True)
    rows, spots = (circle.shape[1], circle.shape[2])
    wide_chans = w_query.shape[0]
    head_dim = wide_chans // HEADS
    weights_all = jnp.stack([w_query, w_key, w_value])
    projected = jnp.einsum("kwc,crp->kwrp", weights_all, circle, precision=HIGH)
    projected = projected.reshape(3, HEADS, head_dim, rows, spots)
    attended = attend(projected, score_scale).reshape(wide_chans, rows, spots)
    mixed = circle + jnp.einsum("cw,wrp->crp", w_out, attended, precision=HIGH)
    mixed3 = jnp.concatenate([shifted(mixed, 1, 0), mixed, shifted(mixed, -1, 0)], axis=1)
    own = summary.shape[2]
    start = (lax.axis_index("lon") * own - 1) % spots
    near = lax.dynamic_slice_in_dim(jnp.concatenate([mixed3, mixed3], axis=2), start, own + 2, 2)
    up_mixed = upsample(near)[:, 2 : 2 + coarse_h + 4, 2 : 2 + wide // 4 + 4]
    joined = jnp.concatenate([up_mixed, coarse], axis=0)
    lifted = inside_rows(jax.nn.silu(convolve(joined, w_up)), 1, coarse_h)
    up_lifted = upsample(lifted)[:, 3 : 3 + height + 2, 3 : 3 + wide + 2]
    return convolve(jnp.concatenate([up_lifted, second], axis=0), w_last)


def solution(mesh):
    placed = (P(None, "lat", "lon"), P(), P(), P(), P(), P(), P(), P(), P(), P(), P())
    return jax.shard_map(
        on_device, mesh=mesh, in_specs=placed, out_specs=P(None, "lat", "lon"), check_vma=False
    )
```

```python
import jax
import jax.numpy as jnp
from jax import lax
from jax.sharding import PartitionSpec as P

HEADS = 8


EPSILON = 1e-06
HIGH = lax.Precision.HIGHEST


def shifted(piece, dlat, dlon):
    n_lat, n_lon = (lax.axis_size("lat"), lax.axis_size("lon"))
    shape = piece.shape
    flat = piece.reshape(-1)
    if dlon == 0:
        pairs = [(a, a + dlat) for a in range(n_lat) if 0 <= a + dlat < n_lat]
        moved = lax.ppermute(flat, "lat", pairs)
    elif dlat == 0:
        pairs = [(b, (b + dlon) % n_lon) for b in range(n_lon)]
        moved = lax.ppermute(flat, "lon", pairs)
    else:
        pairs = [
            (a * n_lon + b, (a + dlat) * n_lon + (b + dlon) % n_lon)
            for a in range(n_lat)
            if 0 <= a + dlat < n_lat
            for b in range(n_lon)
        ]
        moved = lax.ppermute(flat, ("lat", "lon"), pairs)
    return moved.reshape(shape)


def halo(value, lat_width, lon_width):
    _, height, wide = value.shape
    above, below = ([], [])
    for d in range(1, -(-lat_width // height) + 1):
        count = min(height, lat_width - height * (d - 1))
        above.insert(0, shifted(value[:, height - count :, :], d, 0))
        below.append(shifted(value[:, :count, :], -d, 0))
    value = jnp.concatenate(above + [value] + below, axis=1)
    west = shifted(value[:, :, wide - lon_width :], 0, 1)
    east = shifted(value[:, :, :lon_width], 0, -1)
    return jnp.concatenate([west, value, east], axis=2)


def inside_rows(value, width, height):
    first = lax.axis_index("lat") * height - width
    rows = first + lax.broadcasted_iota(jnp.int32, (1, value.shape[1], 1), 1)
    keep = (rows >= 0) & (rows < lax.axis_size("lat") * height)
    return jnp.where(keep, value, 0.0)


def convolve(extended, weight):
    output = lax.conv_general_dilated(
        extended[None],
        weight,
        (1, 1),
        "VALID",
        dimension_numbers=("NCHW", "OIHW", "NCHW"),
        precision=HIGH,
    )
    return output[0]


def pool_cells(values):
    chans, height, width = values.shape
    return values.reshape(chans, height // 4, 4, width // 4, 4).mean(axis=(2, 4))


def upsample(values):
    return jnp.repeat(jnp.repeat(values, 4, axis=1), 4, axis=2)


def attend(stacked, scales):
    query, keys, values = (stacked[0], stacked[1], stacked[2])
    query = query * lax.rsqrt(jnp.mean(query * query, axis=1, keepdims=True) + EPSILON)
    keys = keys * lax.rsqrt(jnp.mean(keys * keys, axis=1, keepdims=True) + EPSILON)
    scores = jnp.einsum("hdri,hdrj->hrij", query, keys, precision=HIGH)
    scores = scores * (scales / query.shape[1])[:, None, None, None]
    weights = jnp.exp(scores)
    weights = weights / jnp.sum(weights, axis=3, keepdims=True)
    return jnp.einsum("hrij,hdrj->hdri", weights, values, precision=HIGH)


def on_device(
    field, w_first, w_second, w_down, w_query, w_key, w_value, w_out, score_scale, w_up, w_last
):
    _, height, wide = field.shape
    coarse_h = height // 4
    first = inside_rows(jax.nn.silu(convolve(halo(field, 3, 3), w_first)), 2, height)
    second = inside_rows(jax.nn.silu(convolve(first, w_second)), 1, height)
    pooled = pool_cells(second[:, 1 : 1 + height, 1 : 1 + wide])
    reach = coarse_h + 1
    coarse = convolve(halo(pooled, reach, 3), w_down)
    coarse = inside_rows(jax.nn.silu(coarse), coarse_h, coarse_h)
    summary = pool_cells(coarse[:, :, 2 : 2 + wide // 4])
    circle = lax.all_gather(summary, "lon", axis=2, tiled=True)
    rows, spots = (circle.shape[1], circle.shape[2])
    wide_chans = w_query.shape[0]
    head_dim = wide_chans // HEADS
    weights_all = jnp.stack([w_query, w_key, w_value])
    projected = jnp.einsum("kwc,crp->kwrp", weights_all, circle, precision=HIGH)
    projected = projected.reshape(3, HEADS, head_dim, rows, spots)
    attended = attend(projected, score_scale).reshape(wide_chans, rows, spots)
    mixed = circle + jnp.einsum("cw,wrp->crp", w_out, attended, precision=HIGH)
    mixed = inside_rows(mixed, 1, 1)
    own = summary.shape[2]
    start = (lax.axis_index("lon") * own - 1) % spots
    near = lax.dynamic_slice_in_dim(jnp.concatenate([mixed, mixed], axis=2), start, own + 2, 2)
    up_mixed = upsample(near)[:, 2 : 2 + coarse_h + 4, 2 : 2 + wide // 4 + 4]
    joined = jnp.concatenate([up_mixed, coarse[:, 2 : 2 + coarse_h + 4]], axis=0)
    lifted = inside_rows(jax.nn.silu(convolve(joined, w_up)), 1, coarse_h)
    up_lifted = upsample(lifted)[:, 3 : 3 + height + 2, 3 : 3 + wide + 2]
    return convolve(jnp.concatenate([up_lifted, second], axis=0), w_last)


def solution(mesh):
    placed = (P(None, "lat", "lon"), P(), P(), P(), P(), P(), P(), P(), P(), P(), P())
    return jax.shard_map(
        on_device, mesh=mesh, in_specs=placed, out_specs=P(None, "lat", "lon"), check_vma=False
    )
```

```python
import jax
import jax.numpy as jnp
from jax import lax
from jax.sharding import PartitionSpec as P

HEADS = 8


EPSILON = 1e-06
HIGH = lax.Precision.HIGHEST
CONV = lax.Precision.HIGH


def shifted(piece, dlat, dlon):
    n_lat, n_lon = (lax.axis_size("lat"), lax.axis_size("lon"))
    shape = piece.shape
    flat = piece.reshape(-1)
    if dlon == 0:
        pairs = [(a, a + dlat) for a in range(n_lat) if 0 <= a + dlat < n_lat]
        moved = lax.ppermute(flat, "lat", pairs)
    elif dlat == 0:
        pairs = [(b, (b + dlon) % n_lon) for b in range(n_lon)]
        moved = lax.ppermute(flat, "lon", pairs)
    else:
        pairs = [
            (a * n_lon + b, (a + dlat) * n_lon + (b + dlon) % n_lon)
            for a in range(n_lat)
            if 0 <= a + dlat < n_lat
            for b in range(n_lon)
        ]
        moved = lax.ppermute(flat, ("lat", "lon"), pairs)
    return moved.reshape(shape)


def halo(value, lat_width, lon_width):
    _, height, wide = value.shape
    above, below = ([], [])
    for d in range(1, -(-lat_width // height) + 1):
        count = min(height, lat_width - height * (d - 1))
        above.insert(0, shifted(value[:, height - count :, :], d, 0))
        below.append(shifted(value[:, :count, :], -d, 0))
    value = jnp.concatenate(above + [value] + below, axis=1)
    west = shifted(value[:, :, wide - lon_width :], 0, 1)
    east = shifted(value[:, :, :lon_width], 0, -1)
    return jnp.concatenate([west, value, east], axis=2)


def inside_rows(value, width, height):
    first = lax.axis_index("lat") * height - width
    rows = first + lax.broadcasted_iota(jnp.int32, (1, value.shape[1], 1), 1)
    keep = (rows >= 0) & (rows < lax.axis_size("lat") * height)
    return jnp.where(keep, value, 0.0)


def convolve(extended, weight):
    output = lax.conv_general_dilated(
        extended[None],
        weight,
        (1, 1),
        "VALID",
        dimension_numbers=("NCHW", "OIHW", "NCHW"),
        precision=CONV,
    )
    return output[0]


def pool_cells(values):
    chans, height, width = values.shape
    return values.reshape(chans, height // 4, 4, width // 4, 4).mean(axis=(2, 4))


def upsample(values):
    return jnp.repeat(jnp.repeat(values, 4, axis=1), 4, axis=2)


def attend(stacked, scales):
    query, keys, values = (stacked[0], stacked[1], stacked[2])
    query = query * lax.rsqrt(jnp.mean(query * query, axis=1, keepdims=True) + EPSILON)
    keys = keys * lax.rsqrt(jnp.mean(keys * keys, axis=1, keepdims=True) + EPSILON)
    scores = jnp.einsum("hdri,hdrj->hrij", query, keys, precision=HIGH)
    scores = scores * (scales / query.shape[1])[:, None, None, None]
    weights = jnp.exp(scores)
    weights = weights / jnp.sum(weights, axis=3, keepdims=True)
    return jnp.einsum("hrij,hdrj->hdri", weights, values, precision=HIGH)


def on_device(
    field, w_first, w_second, w_down, w_query, w_key, w_value, w_out, score_scale, w_up, w_last
):
    _, height, wide = field.shape
    coarse_h = height // 4
    first = inside_rows(jax.nn.silu(convolve(halo(field, 3, 3), w_first)), 2, height)
    second = inside_rows(jax.nn.silu(convolve(first, w_second)), 1, height)
    pooled = pool_cells(second[:, 1 : 1 + height, 1 : 1 + wide])
    reach = coarse_h + 1
    coarse = convolve(halo(pooled, reach, 3), w_down)
    coarse = inside_rows(jax.nn.silu(coarse), coarse_h, coarse_h)
    summary = pool_cells(coarse[:, :, 2 : 2 + wide // 4])
    circle = lax.all_gather(summary, "lon", axis=2, tiled=True)
    rows, spots = (circle.shape[1], circle.shape[2])
    wide_chans = w_query.shape[0]
    head_dim = wide_chans // HEADS
    weights_all = jnp.stack([w_query, w_key, w_value])
    projected = jnp.einsum("kwc,crp->kwrp", weights_all, circle, precision=HIGH)
    projected = projected.reshape(3, HEADS, head_dim, rows, spots)
    attended = attend(projected, score_scale).reshape(wide_chans, rows, spots)
    mixed = circle + jnp.einsum("cw,wrp->crp", w_out, attended, precision=HIGH)
    mixed = inside_rows(mixed, 1, 1)
    own = summary.shape[2]
    start = (lax.axis_index("lon") * own - 1) % spots
    near = lax.dynamic_slice_in_dim(jnp.concatenate([mixed, mixed], axis=2), start, own + 2, 2)
    up_mixed = upsample(near)[:, 2 : 2 + coarse_h + 4, 2 : 2 + wide // 4 + 4]
    joined = jnp.concatenate([up_mixed, coarse[:, 2 : 2 + coarse_h + 4]], axis=0)
    lifted = inside_rows(jax.nn.silu(convolve(joined, w_up)), 1, coarse_h)
    up_lifted = upsample(lifted)[:, 3 : 3 + height + 2, 3 : 3 + wide + 2]
    return convolve(jnp.concatenate([up_lifted, second], axis=0), w_last)


def solution(mesh):
    placed = (P(None, "lat", "lon"), P(), P(), P(), P(), P(), P(), P(), P(), P(), P())
    return jax.shard_map(
        on_device, mesh=mesh, in_specs=placed, out_specs=P(None, "lat", "lon"), check_vma=False
    )
```

```python
import jax
import jax.numpy as jnp
from jax import lax
from jax.sharding import PartitionSpec as P

HEADS = 8


EPSILON = 1e-06
HIGH = lax.Precision.HIGH
CONV = lax.Precision.HIGH


def shifted(piece, dlat, dlon):
    n_lat, n_lon = (lax.axis_size("lat"), lax.axis_size("lon"))
    shape = piece.shape
    flat = piece.reshape(-1)
    if dlon == 0:
        pairs = [(a, a + dlat) for a in range(n_lat) if 0 <= a + dlat < n_lat]
        moved = lax.ppermute(flat, "lat", pairs)
    elif dlat == 0:
        pairs = [(b, (b + dlon) % n_lon) for b in range(n_lon)]
        moved = lax.ppermute(flat, "lon", pairs)
    else:
        pairs = [
            (a * n_lon + b, (a + dlat) * n_lon + (b + dlon) % n_lon)
            for a in range(n_lat)
            if 0 <= a + dlat < n_lat
            for b in range(n_lon)
        ]
        moved = lax.ppermute(flat, ("lat", "lon"), pairs)
    return moved.reshape(shape)


def halo(value, lat_width, lon_width):
    height, wide, _ = value.shape
    above, below = ([], [])
    for d in range(1, -(-lat_width // height) + 1):
        count = min(height, lat_width - height * (d - 1))
        above.insert(0, shifted(value[height - count :], d, 0))
        below.append(shifted(value[:count], -d, 0))
    value = jnp.concatenate(above + [value] + below, axis=0)
    west = shifted(value[:, wide - lon_width :], 0, 1)
    east = shifted(value[:, :lon_width], 0, -1)
    return jnp.concatenate([west, value, east], axis=1)


def inside_rows(value, width, height):
    first = lax.axis_index("lat") * height - width
    rows = first + lax.broadcasted_iota(jnp.int32, (value.shape[0], 1, 1), 0)
    keep = (rows >= 0) & (rows < lax.axis_size("lat") * height)
    return jnp.where(keep, value, 0.0)


def convolve(extended, weight):
    output = lax.conv_general_dilated(
        extended[None],
        weight,
        (1, 1),
        "VALID",
        dimension_numbers=("NHWC", "OIHW", "NHWC"),
        precision=CONV,
    )
    return output[0]


def pool_cells(values):
    height, width, chans = values.shape
    return values.reshape(height // 4, 4, width // 4, 4, chans).mean(axis=(1, 3))


def upsample(values):
    return jnp.repeat(jnp.repeat(values, 4, axis=0), 4, axis=1)


def attend(stacked, scales):
    query, keys, values = (stacked[0], stacked[1], stacked[2])
    query = query * lax.rsqrt(jnp.mean(query * query, axis=1, keepdims=True) + EPSILON)
    keys = keys * lax.rsqrt(jnp.mean(keys * keys, axis=1, keepdims=True) + EPSILON)
    scores = jnp.einsum("hdri,hdrj->hrij", query, keys, precision=HIGH)
    scores = scores * (scales / query.shape[1])[:, None, None, None]
    weights = jnp.exp(scores)
    weights = weights / jnp.sum(weights, axis=3, keepdims=True)
    return jnp.einsum("hrij,hdrj->hdri", weights, values, precision=HIGH)


def on_device(
    field, w_first, w_second, w_down, w_query, w_key, w_value, w_out, score_scale, w_up, w_last
):
    field = jnp.transpose(field, (1, 2, 0))
    height, wide, _ = field.shape
    coarse_h = height // 4
    first = inside_rows(jax.nn.silu(convolve(halo(field, 3, 3), w_first)), 2, height)
    second = inside_rows(jax.nn.silu(convolve(first, w_second)), 1, height)
    pooled = pool_cells(second[1 : 1 + height, 1 : 1 + wide])
    reach = coarse_h + 1
    coarse = convolve(halo(pooled, reach, 3), w_down)
    coarse = inside_rows(jax.nn.silu(coarse), coarse_h, coarse_h)
    summary = pool_cells(coarse[:, 2 : 2 + wide // 4])
    circle = lax.all_gather(summary, "lon", axis=1, tiled=True)
    rows, spots = (circle.shape[0], circle.shape[1])
    wide_chans = w_query.shape[0]
    head_dim = wide_chans // HEADS
    weights_all = jnp.stack([w_query, w_key, w_value])
    projected = jnp.einsum("kwc,rpc->kwrp", weights_all, circle, precision=HIGH)
    projected = projected.reshape(3, HEADS, head_dim, rows, spots)
    attended = attend(projected, score_scale).reshape(wide_chans, rows, spots)
    mixed = circle + jnp.einsum("cw,wrp->rpc", w_out, attended, precision=HIGH)
    mixed = inside_rows(mixed, 1, 1)
    own = summary.shape[1]
    start = (lax.axis_index("lon") * own - 1) % spots
    near = lax.dynamic_slice_in_dim(jnp.concatenate([mixed, mixed], axis=1), start, own + 2, 1)
    up_mixed = upsample(near)[2 : 2 + coarse_h + 4, 2 : 2 + wide // 4 + 4]
    joined = jnp.concatenate([up_mixed, coarse[2 : 2 + coarse_h + 4]], axis=2)
    lifted = inside_rows(jax.nn.silu(convolve(joined, w_up)), 1, coarse_h)
    up_lifted = upsample(lifted)[3 : 3 + height + 2, 3 : 3 + wide + 2]
    result = convolve(jnp.concatenate([up_lifted, second], axis=2), w_last)
    return jnp.transpose(result, (2, 0, 1))


def solution(mesh):
    placed = (P(None, "lat", "lon"), P(), P(), P(), P(), P(), P(), P(), P(), P(), P())
    return jax.shard_map(
        on_device, mesh=mesh, in_specs=placed, out_specs=P(None, "lat", "lon"), check_vma=False
    )
```

```python
import jax
import jax.numpy as jnp
from jax import lax
from jax.sharding import PartitionSpec as P

HEADS = 8


EPSILON = 1e-06
HIGH = lax.Precision.HIGH
CONV = lax.Precision.HIGH


def shifted(piece, dlat, dlon):
    n_lat, n_lon = (lax.axis_size("lat"), lax.axis_size("lon"))
    shape = piece.shape
    flat = piece.reshape(-1)
    if dlon == 0:
        pairs = [(a, a + dlat) for a in range(n_lat) if 0 <= a + dlat < n_lat]
        moved = lax.ppermute(flat, "lat", pairs)
    elif dlat == 0:
        pairs = [(b, (b + dlon) % n_lon) for b in range(n_lon)]
        moved = lax.ppermute(flat, "lon", pairs)
    else:
        pairs = [
            (a * n_lon + b, (a + dlat) * n_lon + (b + dlon) % n_lon)
            for a in range(n_lat)
            if 0 <= a + dlat < n_lat
            for b in range(n_lon)
        ]
        moved = lax.ppermute(flat, ("lat", "lon"), pairs)
    return moved.reshape(shape)


def halo(value, lat_width, lon_width):
    height, wide, _ = value.shape
    above, below = ([], [])
    for d in range(1, -(-lat_width // height) + 1):
        count = min(height, lat_width - height * (d - 1))
        above.insert(0, shifted(value[height - count :], d, 0))
        below.append(shifted(value[:count], -d, 0))
    value = jnp.concatenate(above + [value] + below, axis=0)
    west = shifted(value[:, wide - lon_width :], 0, 1)
    east = shifted(value[:, :lon_width], 0, -1)
    return jnp.concatenate([west, value, east], axis=1)


def inside_rows(value, width, height):
    first = lax.axis_index("lat") * height - width
    rows = first + lax.broadcasted_iota(jnp.int32, (value.shape[0], 1, 1), 0)
    keep = (rows >= 0) & (rows < lax.axis_size("lat") * height)
    return jnp.where(keep, value, 0.0)


def convolve(extended, weight):
    output = lax.conv_general_dilated(
        extended[None],
        weight,
        (1, 1),
        "VALID",
        dimension_numbers=("NHWC", "OIHW", "NHWC"),
        precision=CONV,
    )
    return output[0]


def pool_cells(values):
    height, width, chans = values.shape
    return values.reshape(height // 4, 4, width // 4, 4, chans).mean(axis=(1, 3))


def upsample(values):
    return jnp.repeat(jnp.repeat(values, 4, axis=0), 4, axis=1)


def attend(stacked, scales):
    query, keys, values = (stacked[0], stacked[1], stacked[2])
    query = query * lax.rsqrt(jnp.mean(query * query, axis=1, keepdims=True) + EPSILON)
    keys = keys * lax.rsqrt(jnp.mean(keys * keys, axis=1, keepdims=True) + EPSILON)
    scores = jnp.einsum("hdri,hdrj->hrij", query, keys, precision=HIGH)
    scores = scores * (scales / query.shape[1])[:, None, None, None]
    weights = jnp.exp(scores)
    weights = weights / jnp.sum(weights, axis=3, keepdims=True)
    return jnp.einsum("hrij,hdrj->hdri", weights, values, precision=HIGH)


def on_device(
    field, w_first, w_second, w_down, w_query, w_key, w_value, w_out, score_scale, w_up, w_last
):
    field = jnp.transpose(field, (1, 2, 0))
    height, wide, _ = field.shape
    coarse_h = height // 4
    first = inside_rows(jax.nn.silu(convolve(halo(field, 3, 3), w_first)), 2, height)
    second = inside_rows(jax.nn.silu(convolve(first, w_second)), 1, height)
    pooled = pool_cells(second[1 : 1 + height, 1 : 1 + wide])
    reach = coarse_h + 1
    coarse = convolve(halo(pooled, reach, 3), w_down)
    coarse = inside_rows(jax.nn.silu(coarse), coarse_h, coarse_h)
    summary = pool_cells(coarse[:, 2 : 2 + wide // 4])
    circle = lax.all_gather(summary, "lon", axis=1, tiled=True)
    rows, spots = (circle.shape[0], circle.shape[1])
    wide_chans = w_query.shape[0]
    head_dim = wide_chans // HEADS
    weights_all = jnp.stack([w_query, w_key, w_value])
    projected = jnp.einsum("kwc,rpc->kwrp", weights_all, circle, precision=HIGH)
    projected = projected.reshape(3, HEADS, head_dim, rows, spots)
    attended = attend(projected, score_scale).reshape(wide_chans, rows, spots)
    mixed = circle + jnp.einsum("cw,wrp->rpc", w_out, attended, precision=HIGH)
    mixed = inside_rows(mixed, 1, 1)
    own = summary.shape[1]
    start = (lax.axis_index("lon") * own - 1) % spots
    near = lax.dynamic_slice_in_dim(jnp.concatenate([mixed, mixed], axis=1), start, own + 2, 1)
    up_mixed = upsample(near)[2 : 2 + coarse_h + 4, 2 : 2 + wide // 4 + 4]
    joined = jnp.concatenate([up_mixed, coarse[2 : 2 + coarse_h + 4]], axis=2)
    lifted = inside_rows(jax.nn.silu(convolve(joined, w_up)), 1, coarse_h)
    up_lifted = upsample(lifted)[3 : 3 + height + 2, 3 : 3 + wide + 2]
    split = up_lifted.shape[2]
    result = convolve(up_lifted, w_last[:, :split]) + convolve(second, w_last[:, split:])
    return jnp.transpose(result, (2, 0, 1))


def solution(mesh):
    placed = (P(None, "lat", "lon"), P(), P(), P(), P(), P(), P(), P(), P(), P(), P())
    return jax.shard_map(
        on_device, mesh=mesh, in_specs=placed, out_specs=P(None, "lat", "lon"), check_vma=False
    )
```

```python
import jax
import jax.numpy as jnp
from jax import lax
from jax.sharding import PartitionSpec as P

HEADS = 8


EPSILON = 1e-06
HIGH = lax.Precision.HIGH
CONV = lax.Precision.HIGH


def shifted(piece, dlat, dlon):
    n_lat, n_lon = (lax.axis_size("lat"), lax.axis_size("lon"))
    shape = piece.shape
    flat = piece.reshape(-1)
    if dlon == 0:
        pairs = [(a, a + dlat) for a in range(n_lat) if 0 <= a + dlat < n_lat]
        moved = lax.ppermute(flat, "lat", pairs)
    elif dlat == 0:
        pairs = [(b, (b + dlon) % n_lon) for b in range(n_lon)]
        moved = lax.ppermute(flat, "lon", pairs)
    else:
        pairs = [
            (a * n_lon + b, (a + dlat) * n_lon + (b + dlon) % n_lon)
            for a in range(n_lat)
            if 0 <= a + dlat < n_lat
            for b in range(n_lon)
        ]
        moved = lax.ppermute(flat, ("lat", "lon"), pairs)
    return moved.reshape(shape)


def halo(value, lat_width, lon_width):
    height, wide, _ = value.shape
    above, below = ([], [])
    for d in range(1, -(-lat_width // height) + 1):
        count = min(height, lat_width - height * (d - 1))
        above.insert(0, shifted(value[height - count :], d, 0))
        below.append(shifted(value[:count], -d, 0))
    value = jnp.concatenate(above + [value] + below, axis=0)
    west = shifted(value[:, wide - lon_width :], 0, 1)
    east = shifted(value[:, :lon_width], 0, -1)
    return jnp.concatenate([west, value, east], axis=1)


def inside_rows(value, width, height):
    first = lax.axis_index("lat") * height - width
    rows = first + lax.broadcasted_iota(jnp.int32, (value.shape[0], 1, 1), 0)
    keep = (rows >= 0) & (rows < lax.axis_size("lat") * height)
    return jnp.where(keep, value, 0.0)


def convolve(extended, weight):
    output = lax.conv_general_dilated(
        extended[None],
        weight,
        (1, 1),
        "VALID",
        dimension_numbers=("NHWC", "OIHW", "NHWC"),
        precision=CONV,
    )
    return output[0]


def pool_cells(values):
    height, width, chans = values.shape
    return values.reshape(height // 4, 4, width // 4, 4, chans).mean(axis=(1, 3))


def upsample(values):
    return jnp.repeat(jnp.repeat(values, 4, axis=0), 4, axis=1)


def attend(stacked, scales):
    query, keys, values = (stacked[0], stacked[1], stacked[2])
    query = query * lax.rsqrt(jnp.mean(query * query, axis=1, keepdims=True) + EPSILON)
    keys = keys * lax.rsqrt(jnp.mean(keys * keys, axis=1, keepdims=True) + EPSILON)
    scores = jnp.einsum("hdri,hdrj->hrij", query, keys, precision=HIGH)
    scores = scores * (scales / query.shape[1])[:, None, None, None]
    weights = jnp.exp(scores)
    weights = weights / jnp.sum(weights, axis=3, keepdims=True)
    return jnp.einsum("hrij,hdrj->hdri", weights, values, precision=HIGH)


def on_device(
    field, w_first, w_second, w_down, w_query, w_key, w_value, w_out, score_scale, w_up, w_last
):
    field = jnp.transpose(field, (1, 2, 0))
    height, wide, _ = field.shape
    coarse_h = height // 4
    first = inside_rows(jax.nn.silu(convolve(halo(field, 3, 3), w_first)), 2, height)
    second = inside_rows(jax.nn.silu(convolve(first, w_second)), 1, height)
    pooled = pool_cells(second[1 : 1 + height, 1 : 1 + wide])
    reach = coarse_h + 1
    split = w_last.shape[1] - second.shape[2]
    skip = convolve(second, w_last[:, split:])
    pooled_ext, skip = lax.optimization_barrier((halo(pooled, reach, 3), skip))
    coarse = convolve(pooled_ext, w_down)
    coarse = inside_rows(jax.nn.silu(coarse), coarse_h, coarse_h)
    summary = pool_cells(coarse[:, 2 : 2 + wide // 4])
    circle = lax.all_gather(summary, "lon", axis=1, tiled=True)
    rows, spots = (circle.shape[0], circle.shape[1])
    wide_chans = w_query.shape[0]
    head_dim = wide_chans // HEADS
    weights_all = jnp.stack([w_query, w_key, w_value])
    projected = jnp.einsum("kwc,rpc->kwrp", weights_all, circle, precision=HIGH)
    projected = projected.reshape(3, HEADS, head_dim, rows, spots)
    attended = attend(projected, score_scale).reshape(wide_chans, rows, spots)
    mixed = circle + jnp.einsum("cw,wrp->rpc", w_out, attended, precision=HIGH)
    mixed = inside_rows(mixed, 1, 1)
    own = summary.shape[1]
    start = (lax.axis_index("lon") * own - 1) % spots
    near = lax.dynamic_slice_in_dim(jnp.concatenate([mixed, mixed], axis=1), start, own + 2, 1)
    up_mixed = upsample(near)[2 : 2 + coarse_h + 4, 2 : 2 + wide // 4 + 4]
    joined = jnp.concatenate([up_mixed, coarse[2 : 2 + coarse_h + 4]], axis=2)
    lifted = inside_rows(jax.nn.silu(convolve(joined, w_up)), 1, coarse_h)
    up_lifted = upsample(lifted)[3 : 3 + height + 2, 3 : 3 + wide + 2]
    result = convolve(up_lifted, w_last[:, :split]) + skip
    return jnp.transpose(result, (2, 0, 1))


def solution(mesh):
    placed = (P(None, "lat", "lon"), P(), P(), P(), P(), P(), P(), P(), P(), P(), P())
    return jax.shard_map(
        on_device, mesh=mesh, in_specs=placed, out_specs=P(None, "lat", "lon"), check_vma=False
    )
```

```python
import jax
import jax.numpy as jnp
from jax import lax
from jax.sharding import PartitionSpec as P

HEADS = 8


EPSILON = 1e-06
HIGH = lax.Precision.HIGH
CONV = lax.Precision.HIGH


def shifted(piece, dlat, dlon):
    n_lat, n_lon = (lax.axis_size("lat"), lax.axis_size("lon"))
    shape = piece.shape
    flat = piece.reshape(-1)
    if dlon == 0:
        pairs = [(a, a + dlat) for a in range(n_lat) if 0 <= a + dlat < n_lat]
        moved = lax.ppermute(flat, "lat", pairs)
    elif dlat == 0:
        pairs = [(b, (b + dlon) % n_lon) for b in range(n_lon)]
        moved = lax.ppermute(flat, "lon", pairs)
    else:
        pairs = [
            (a * n_lon + b, (a + dlat) * n_lon + (b + dlon) % n_lon)
            for a in range(n_lat)
            if 0 <= a + dlat < n_lat
            for b in range(n_lon)
        ]
        moved = lax.ppermute(flat, ("lat", "lon"), pairs)
    return moved.reshape(shape)


def halo(value, lat_width, lon_width):
    height, wide, _ = value.shape
    above, below = ([], [])
    for d in range(1, -(-lat_width // height) + 1):
        count = min(height, lat_width - height * (d - 1))
        above.insert(0, shifted(value[height - count :], d, 0))
        below.append(shifted(value[:count], -d, 0))
    value = jnp.concatenate(above + [value] + below, axis=0)
    west = shifted(value[:, wide - lon_width :], 0, 1)
    east = shifted(value[:, :lon_width], 0, -1)
    return jnp.concatenate([west, value, east], axis=1)


def inside_rows(value, width, height):
    first = lax.axis_index("lat") * height - width
    rows = first + lax.broadcasted_iota(jnp.int32, (value.shape[0], 1, 1), 0)
    keep = (rows >= 0) & (rows < lax.axis_size("lat") * height)
    return jnp.where(keep, value, 0.0)


def convolve(extended, weight):
    output = lax.conv_general_dilated(
        extended[None],
        weight,
        (1, 1),
        "VALID",
        dimension_numbers=("NHWC", "OIHW", "NHWC"),
        precision=CONV,
    )
    return output[0]


def pool_cells(values):
    height, width, chans = values.shape
    return values.reshape(height // 4, 4, width // 4, 4, chans).mean(axis=(1, 3))


def upsample(values):
    return jnp.repeat(jnp.repeat(values, 4, axis=0), 4, axis=1)


def attend(stacked, scales):
    query, keys, values = (stacked[0], stacked[1], stacked[2])
    query = query * lax.rsqrt(jnp.mean(query * query, axis=1, keepdims=True) + EPSILON)
    keys = keys * lax.rsqrt(jnp.mean(keys * keys, axis=1, keepdims=True) + EPSILON)
    scores = jnp.einsum("hdri,hdrj->hrij", query, keys, precision=HIGH)
    scores = scores * (scales / query.shape[1])[:, None, None, None]
    weights = jnp.exp(scores)
    weights = weights / jnp.sum(weights, axis=3, keepdims=True)
    return jnp.einsum("hrij,hdrj->hdri", weights, values, precision=HIGH)


def on_device(
    field, w_first, w_second, w_down, w_query, w_key, w_value, w_out, score_scale, w_up, w_last
):
    field = jnp.transpose(field, (1, 2, 0))
    height, wide, _ = field.shape
    coarse_h = height // 4
    first = inside_rows(jax.nn.silu(convolve(halo(field, 3, 3), w_first)), 2, height)
    second = inside_rows(jax.nn.silu(convolve(first, w_second)), 1, height)
    pooled = pool_cells(second[1 : 1 + height, 1 : 1 + wide])
    reach = coarse_h + 1
    split = w_last.shape[1] - second.shape[2]
    skip = convolve(second, w_last[:, split:])
    pooled_ext, skip = lax.optimization_barrier((halo(pooled, reach, 3), skip))
    coarse = convolve(pooled_ext, w_down)
    coarse = inside_rows(jax.nn.silu(coarse), coarse_h, coarse_h)
    summary = pool_cells(coarse[:, 2 : 2 + wide // 4])
    n_lon = lax.axis_size("lon")
    sent = jnp.tile(summary, (n_lon, 1, 1))
    got = lax.all_to_all(sent, "lon", 0, 0, tiled=True).reshape((n_lon,) + summary.shape)
    circle = jnp.transpose(got, (1, 0, 2, 3)).reshape(summary.shape[0], -1, summary.shape[2])
    rows, spots = (circle.shape[0], circle.shape[1])
    wide_chans = w_query.shape[0]
    head_dim = wide_chans // HEADS
    weights_all = jnp.stack([w_query, w_key, w_value])
    projected = jnp.einsum("kwc,rpc->kwrp", weights_all, circle, precision=HIGH)
    projected = projected.reshape(3, HEADS, head_dim, rows, spots)
    attended = attend(projected, score_scale).reshape(wide_chans, rows, spots)
    mixed = circle + jnp.einsum("cw,wrp->rpc", w_out, attended, precision=HIGH)
    mixed = inside_rows(mixed, 1, 1)
    own = summary.shape[1]
    start = (lax.axis_index("lon") * own - 1) % spots
    near = lax.dynamic_slice_in_dim(jnp.concatenate([mixed, mixed], axis=1), start, own + 2, 1)
    up_mixed = upsample(near)[2 : 2 + coarse_h + 4, 2 : 2 + wide // 4 + 4]
    joined = jnp.concatenate([up_mixed, coarse[2 : 2 + coarse_h + 4]], axis=2)
    lifted = inside_rows(jax.nn.silu(convolve(joined, w_up)), 1, coarse_h)
    up_lifted = upsample(lifted)[3 : 3 + height + 2, 3 : 3 + wide + 2]
    result = convolve(up_lifted, w_last[:, :split]) + skip
    return jnp.transpose(result, (2, 0, 1))


def solution(mesh):
    placed = (P(None, "lat", "lon"), P(), P(), P(), P(), P(), P(), P(), P(), P(), P())
    return jax.shard_map(
        on_device, mesh=mesh, in_specs=placed, out_specs=P(None, "lat", "lon"), check_vma=False
    )
```

```python
import jax
import jax.numpy as jnp
from jax import lax
from jax.sharding import PartitionSpec as P

HEADS = 8


EPSILON = 1e-06
HIGH = lax.Precision.HIGH
CONV = lax.Precision.HIGH


def shifted(piece, dlat, dlon):
    n_lat, n_lon = (lax.axis_size("lat"), lax.axis_size("lon"))
    shape = piece.shape
    flat = piece.reshape(-1)
    if dlon == 0:
        pairs = [(a, a + dlat) for a in range(n_lat) if 0 <= a + dlat < n_lat]
        moved = lax.ppermute(flat, "lat", pairs)
    elif dlat == 0:
        pairs = [(b, (b + dlon) % n_lon) for b in range(n_lon)]
        moved = lax.ppermute(flat, "lon", pairs)
    else:
        pairs = [
            (a * n_lon + b, (a + dlat) * n_lon + (b + dlon) % n_lon)
            for a in range(n_lat)
            if 0 <= a + dlat < n_lat
            for b in range(n_lon)
        ]
        moved = lax.ppermute(flat, ("lat", "lon"), pairs)
    return moved.reshape(shape)


def halo(value, lat_width, lon_width):
    height, wide, _ = value.shape
    above, below = ([], [])
    for d in range(1, -(-lat_width // height) + 1):
        count = min(height, lat_width - height * (d - 1))
        above.insert(0, shifted(value[height - count :], d, 0))
        below.append(shifted(value[:count], -d, 0))
    value = jnp.concatenate(above + [value] + below, axis=0)
    west = shifted(value[:, wide - lon_width :], 0, 1)
    east = shifted(value[:, :lon_width], 0, -1)
    return jnp.concatenate([west, value, east], axis=1)


def inside_rows(value, width, height):
    first = lax.axis_index("lat") * height - width
    rows = first + lax.broadcasted_iota(jnp.int32, (value.shape[0], 1, 1), 0)
    keep = (rows >= 0) & (rows < lax.axis_size("lat") * height)
    return jnp.where(keep, value, 0.0)


def convolve(extended, weight):
    output = lax.conv_general_dilated(
        extended[None],
        weight,
        (1, 1),
        "VALID",
        dimension_numbers=("NHWC", "OIHW", "NHWC"),
        precision=CONV,
    )
    return output[0]


def pool_cells(values):
    height, width, chans = values.shape
    return values.reshape(height // 4, 4, width // 4, 4, chans).mean(axis=(1, 3))


def upsample(values):
    return jnp.repeat(jnp.repeat(values, 4, axis=0), 4, axis=1)


def attend(stacked, scales):
    query, keys, values = (stacked[0], stacked[1], stacked[2])
    query = query * lax.rsqrt(jnp.mean(query * query, axis=1, keepdims=True) + EPSILON)
    keys = keys * lax.rsqrt(jnp.mean(keys * keys, axis=1, keepdims=True) + EPSILON)
    scores = jnp.einsum("hdri,hdrj->hrij", query, keys, precision=HIGH)
    scores = scores * (scales / query.shape[1])[:, None, None, None]
    weights = jnp.exp(scores)
    weights = weights / jnp.sum(weights, axis=3, keepdims=True)
    return jnp.einsum("hrij,hdrj->hdri", weights, values, precision=HIGH)


def on_device(
    field, w_first, w_second, w_down, w_query, w_key, w_value, w_out, score_scale, w_up, w_last
):
    field = jnp.transpose(field, (1, 2, 0))
    height, wide, _ = field.shape
    coarse_h = height // 4
    first = inside_rows(jax.nn.silu(convolve(halo(field, 3, 3), w_first)), 2, height)
    second = inside_rows(jax.nn.silu(convolve(first, w_second)), 1, height)
    pooled = pool_cells(second[1 : 1 + height, 1 : 1 + wide])
    reach = coarse_h + 1
    split = w_last.shape[1] - second.shape[2]
    skip = convolve(second, w_last[:, split:])
    pooled_ext, skip = lax.optimization_barrier((halo(pooled, reach, 3), skip))
    coarse = convolve(pooled_ext, w_down)
    coarse = inside_rows(jax.nn.silu(coarse), coarse_h, coarse_h)
    summary = pool_cells(coarse[:, 2 : 2 + wide // 4])
    n_lon = lax.axis_size("lon")
    sent = jnp.tile(summary, (n_lon, 1, 1))
    got = lax.all_to_all(sent, "lon", 0, 0, tiled=True).reshape((n_lon,) + summary.shape)
    half = w_up.shape[1] - coarse.shape[2]
    coarse_part = convolve(coarse[2 : 2 + coarse_h + 4], w_up[:, half:])
    got, coarse_part = lax.optimization_barrier((got, coarse_part))
    circle = jnp.transpose(got, (1, 0, 2, 3)).reshape(summary.shape[0], -1, summary.shape[2])
    rows, spots = (circle.shape[0], circle.shape[1])
    wide_chans = w_query.shape[0]
    head_dim = wide_chans // HEADS
    weights_all = jnp.stack([w_query, w_key, w_value])
    projected = jnp.einsum("kwc,rpc->kwrp", weights_all, circle, precision=HIGH)
    projected = projected.reshape(3, HEADS, head_dim, rows, spots)
    attended = attend(projected, score_scale).reshape(wide_chans, rows, spots)
    mixed = circle + jnp.einsum("cw,wrp->rpc", w_out, attended, precision=HIGH)
    mixed = inside_rows(mixed, 1, 1)
    own = summary.shape[1]
    start = (lax.axis_index("lon") * own - 1) % spots
    near = lax.dynamic_slice_in_dim(jnp.concatenate([mixed, mixed], axis=1), start, own + 2, 1)
    up_mixed = upsample(near)[2 : 2 + coarse_h + 4, 2 : 2 + wide // 4 + 4]
    lifted = convolve(up_mixed, w_up[:, :half]) + coarse_part
    lifted = inside_rows(jax.nn.silu(lifted), 1, coarse_h)
    up_lifted = upsample(lifted)[3 : 3 + height + 2, 3 : 3 + wide + 2]
    result = convolve(up_lifted, w_last[:, :split]) + skip
    return jnp.transpose(result, (2, 0, 1))


def solution(mesh):
    placed = (P(None, "lat", "lon"), P(), P(), P(), P(), P(), P(), P(), P(), P(), P())
    return jax.shard_map(
        on_device, mesh=mesh, in_specs=placed, out_specs=P(None, "lat", "lon"), check_vma=False
    )
```

```python
import jax
import jax.numpy as jnp
from jax import lax
from jax.sharding import PartitionSpec as P

HEADS = 8


EPSILON = 1e-06
HIGH = lax.Precision.HIGH
CONV = lax.Precision.HIGH


def shifted(piece, dlat, dlon):
    n_lat, n_lon = (lax.axis_size("lat"), lax.axis_size("lon"))
    shape = piece.shape
    flat = piece.reshape(-1)
    if dlon == 0:
        pairs = [(a, a + dlat) for a in range(n_lat) if 0 <= a + dlat < n_lat]
        moved = lax.ppermute(flat, "lat", pairs)
    elif dlat == 0:
        pairs = [(b, (b + dlon) % n_lon) for b in range(n_lon)]
        moved = lax.ppermute(flat, "lon", pairs)
    else:
        pairs = [
            (a * n_lon + b, (a + dlat) * n_lon + (b + dlon) % n_lon)
            for a in range(n_lat)
            if 0 <= a + dlat < n_lat
            for b in range(n_lon)
        ]
        moved = lax.ppermute(flat, ("lat", "lon"), pairs)
    return moved.reshape(shape)


def halo(value, lat_width, lon_width):
    height, wide, _ = value.shape
    above, below = ([], [])
    for d in range(1, -(-lat_width // height) + 1):
        count = min(height, lat_width - height * (d - 1))
        above.insert(0, shifted(value[height - count :], d, 0))
        below.append(shifted(value[:count], -d, 0))
    value = jnp.concatenate(above + [value] + below, axis=0)
    west = shifted(value[:, wide - lon_width :], 0, 1)
    east = shifted(value[:, :lon_width], 0, -1)
    return jnp.concatenate([west, value, east], axis=1)


def inside_rows(value, width, height):
    first = lax.axis_index("lat") * height - width
    rows = first + lax.broadcasted_iota(jnp.int32, (value.shape[0], 1, 1), 0)
    keep = (rows >= 0) & (rows < lax.axis_size("lat") * height)
    return jnp.where(keep, value, 0.0)


def convolve(extended, weight):
    output = lax.conv_general_dilated(
        extended[None],
        weight,
        (1, 1),
        "VALID",
        dimension_numbers=("NHWC", "OIHW", "NHWC"),
        precision=CONV,
    )
    return output[0]


def pool_cells(values):
    height, width, chans = values.shape
    return values.reshape(height // 4, 4, width // 4, 4, chans).mean(axis=(1, 3))


def upsample(values):
    return jnp.repeat(jnp.repeat(values, 4, axis=0), 4, axis=1)


def attend(stacked, scales):
    query, keys, values = (stacked[0], stacked[1], stacked[2])
    query = query * lax.rsqrt(jnp.mean(query * query, axis=1, keepdims=True) + EPSILON)
    keys = keys * lax.rsqrt(jnp.mean(keys * keys, axis=1, keepdims=True) + EPSILON)
    scores = jnp.einsum("hdri,hdrj->hrij", query, keys, precision=HIGH)
    scores = scores * (scales / query.shape[1])[:, None, None, None]
    weights = jnp.exp(scores)
    weights = weights / jnp.sum(weights, axis=3, keepdims=True)
    return jnp.einsum("hrij,hdrj->hdri", weights, values, precision=HIGH)


def on_device(
    field, w_first, w_second, w_down, w_query, w_key, w_value, w_out, score_scale, w_up, w_last
):
    field = jnp.transpose(field, (1, 2, 0))
    height, wide, _ = field.shape
    coarse_h = height // 4
    lat_ext = halo(field, 3, 0)
    ring = 3
    west = shifted(lat_ext[:, wide - ring :], 0, 1)
    east = shifted(lat_ext[:, :ring], 0, -1)
    inner = convolve(jnp.pad(lat_ext, ((0, 0), (ring, ring), (0, 0))), w_first)
    west, east, inner = lax.optimization_barrier((west, east, inner))
    gap = jnp.zeros((lat_ext.shape[0], 2, lat_ext.shape[2]), lat_ext.dtype)
    left = convolve(jnp.concatenate([west, gap], axis=1), w_first)
    right = convolve(jnp.concatenate([gap, east], axis=1), w_first)
    edge = inner.shape[1] - left.shape[1]
    total = inner + jnp.pad(left, ((0, 0), (0, edge), (0, 0))) + jnp.pad(right, ((0, 0), (edge, 0), (0, 0)))
    first = inside_rows(jax.nn.silu(total), 2, height)
    second = inside_rows(jax.nn.silu(convolve(first, w_second)), 1, height)
    pooled = pool_cells(second[1 : 1 + height, 1 : 1 + wide])
    reach = coarse_h + 1
    split = w_last.shape[1] - second.shape[2]
    skip = convolve(second, w_last[:, split:])
    pooled_ext, skip = lax.optimization_barrier((halo(pooled, reach, 3), skip))
    coarse = convolve(pooled_ext, w_down)
    coarse = inside_rows(jax.nn.silu(coarse), coarse_h, coarse_h)
    summary = pool_cells(coarse[:, 2 : 2 + wide // 4])
    n_lon = lax.axis_size("lon")
    sent = jnp.tile(summary, (n_lon, 1, 1))
    got = lax.all_to_all(sent, "lon", 0, 0, tiled=True).reshape((n_lon,) + summary.shape)
    half = w_up.shape[1] - coarse.shape[2]
    coarse_part = convolve(coarse[2 : 2 + coarse_h + 4], w_up[:, half:])
    got, coarse_part = lax.optimization_barrier((got, coarse_part))
    circle = jnp.transpose(got, (1, 0, 2, 3)).reshape(summary.shape[0], -1, summary.shape[2])
    rows, spots = (circle.shape[0], circle.shape[1])
    wide_chans = w_query.shape[0]
    head_dim = wide_chans // HEADS
    weights_all = jnp.stack([w_query, w_key, w_value])
    projected = jnp.einsum("kwc,rpc->kwrp", weights_all, circle, precision=HIGH)
    projected = projected.reshape(3, HEADS, head_dim, rows, spots)
    attended = attend(projected, score_scale).reshape(wide_chans, rows, spots)
    mixed = circle + jnp.einsum("cw,wrp->rpc", w_out, attended, precision=HIGH)
    mixed = inside_rows(mixed, 1, 1)
    own = summary.shape[1]
    start = (lax.axis_index("lon") * own - 1) % spots
    near = lax.dynamic_slice_in_dim(jnp.concatenate([mixed, mixed], axis=1), start, own + 2, 1)
    up_mixed = upsample(near)[2 : 2 + coarse_h + 4, 2 : 2 + wide // 4 + 4]
    lifted = convolve(up_mixed, w_up[:, :half]) + coarse_part
    lifted = inside_rows(jax.nn.silu(lifted), 1, coarse_h)
    up_lifted = upsample(lifted)[3 : 3 + height + 2, 3 : 3 + wide + 2]
    result = convolve(up_lifted, w_last[:, :split]) + skip
    return jnp.transpose(result, (2, 0, 1))


def solution(mesh):
    placed = (P(None, "lat", "lon"), P(), P(), P(), P(), P(), P(), P(), P(), P(), P())
    return jax.shard_map(
        on_device, mesh=mesh, in_specs=placed, out_specs=P(None, "lat", "lon"), check_vma=False
    )
```

```python
import jax
import jax.numpy as jnp
from jax import lax
from jax.sharding import PartitionSpec as P

HEADS = 8


EPSILON = 1e-06
HIGH = lax.Precision.HIGH
CONV = lax.Precision.HIGH


def shifted(piece, dlat, dlon):
    n_lat, n_lon = (lax.axis_size("lat"), lax.axis_size("lon"))
    shape = piece.shape
    flat = piece.reshape(-1)
    if dlon == 0:
        pairs = [(a, a + dlat) for a in range(n_lat) if 0 <= a + dlat < n_lat]
        moved = lax.ppermute(flat, "lat", pairs)
    elif dlat == 0:
        pairs = [(b, (b + dlon) % n_lon) for b in range(n_lon)]
        moved = lax.ppermute(flat, "lon", pairs)
    else:
        pairs = [
            (a * n_lon + b, (a + dlat) * n_lon + (b + dlon) % n_lon)
            for a in range(n_lat)
            if 0 <= a + dlat < n_lat
            for b in range(n_lon)
        ]
        moved = lax.ppermute(flat, ("lat", "lon"), pairs)
    return moved.reshape(shape)


def halo(value, lat_width, lon_width):
    height, wide, _ = value.shape
    above, below = ([], [])
    for d in range(1, -(-lat_width // height) + 1):
        count = min(height, lat_width - height * (d - 1))
        above.insert(0, shifted(value[height - count :], d, 0))
        below.append(shifted(value[:count], -d, 0))
    value = jnp.concatenate(above + [value] + below, axis=0)
    west = shifted(value[:, wide - lon_width :], 0, 1)
    east = shifted(value[:, :lon_width], 0, -1)
    return jnp.concatenate([west, value, east], axis=1)


def inside_rows(value, width, height):
    first = lax.axis_index("lat") * height - width
    rows = first + lax.broadcasted_iota(jnp.int32, (value.shape[0], 1, 1), 0)
    keep = (rows >= 0) & (rows < lax.axis_size("lat") * height)
    return jnp.where(keep, value, 0.0)


def convolve(extended, weight):
    output = lax.conv_general_dilated(
        extended[None],
        weight,
        (1, 1),
        "VALID",
        dimension_numbers=("NHWC", "OIHW", "NHWC"),
        precision=CONV,
    )
    return output[0]


def pool_cells(values):
    height, width, chans = values.shape
    return values.reshape(height // 4, 4, width // 4, 4, chans).mean(axis=(1, 3))


def upsample(values):
    return jnp.repeat(jnp.repeat(values, 4, axis=0), 4, axis=1)


def attend(stacked, scales):
    query, keys, values = (stacked[0], stacked[1], stacked[2])
    query = query * lax.rsqrt(jnp.mean(query * query, axis=1, keepdims=True) + EPSILON)
    keys = keys * lax.rsqrt(jnp.mean(keys * keys, axis=1, keepdims=True) + EPSILON)
    scores = jnp.einsum("hdri,hdrj->hrij", query, keys, precision=HIGH)
    scores = scores * (scales / query.shape[1])[:, None, None, None]
    weights = jnp.exp(scores)
    weights = weights / jnp.sum(weights, axis=3, keepdims=True)
    return jnp.einsum("hrij,hdrj->hdri", weights, values, precision=HIGH)


def on_device(
    field, w_first, w_second, w_down, w_query, w_key, w_value, w_out, score_scale, w_up, w_last
):
    _, height, wide = field.shape
    coarse_h = height // 4
    above = jnp.transpose(shifted(field[:, height - 3 :], 1, 0), (1, 2, 0))
    below = jnp.transpose(shifted(field[:, :3], -1, 0), (1, 2, 0))
    rows = jnp.concatenate([above, jnp.transpose(field, (1, 2, 0)), below], axis=0)
    west = shifted(rows[:, wide - 3 :], 0, 1)
    east = shifted(rows[:, :3], 0, -1)
    field_ext = jnp.concatenate([west, rows, east], axis=1)
    first = inside_rows(jax.nn.silu(convolve(field_ext, w_first)), 2, height)
    second = inside_rows(jax.nn.silu(convolve(first, w_second)), 1, height)
    pooled = pool_cells(second[1 : 1 + height, 1 : 1 + wide])
    reach = coarse_h + 1
    split = w_last.shape[1] - second.shape[2]
    skip = convolve(second, w_last[:, split:])
    pooled_ext, skip = lax.optimization_barrier((halo(pooled, reach, 3), skip))
    coarse = convolve(pooled_ext, w_down)
    coarse = inside_rows(jax.nn.silu(coarse), coarse_h, coarse_h)
    summary = pool_cells(coarse[:, 2 : 2 + wide // 4])
    n_lon = lax.axis_size("lon")
    sent = jnp.tile(summary, (n_lon, 1, 1))
    got = lax.all_to_all(sent, "lon", 0, 0, tiled=True).reshape((n_lon,) + summary.shape)
    half = w_up.shape[1] - coarse.shape[2]
    coarse_part = convolve(coarse[2 : 2 + coarse_h + 4], w_up[:, half:])
    got, coarse_part = lax.optimization_barrier((got, coarse_part))
    circle = jnp.transpose(got, (1, 0, 2, 3)).reshape(summary.shape[0], -1, summary.shape[2])
    rows, spots = (circle.shape[0], circle.shape[1])
    wide_chans = w_query.shape[0]
    head_dim = wide_chans // HEADS
    weights_all = jnp.stack([w_query, w_key, w_value])
    projected = jnp.einsum("kwc,rpc->kwrp", weights_all, circle, precision=HIGH)
    projected = projected.reshape(3, HEADS, head_dim, rows, spots)
    attended = attend(projected, score_scale).reshape(wide_chans, rows, spots)
    mixed = circle + jnp.einsum("cw,wrp->rpc", w_out, attended, precision=HIGH)
    mixed = inside_rows(mixed, 1, 1)
    own = summary.shape[1]
    start = (lax.axis_index("lon") * own - 1) % spots
    near = lax.dynamic_slice_in_dim(jnp.concatenate([mixed, mixed], axis=1), start, own + 2, 1)
    up_mixed = upsample(near)[2 : 2 + coarse_h + 4, 2 : 2 + wide // 4 + 4]
    lifted = convolve(up_mixed, w_up[:, :half]) + coarse_part
    lifted = inside_rows(jax.nn.silu(lifted), 1, coarse_h)
    up_lifted = upsample(lifted)[3 : 3 + height + 2, 3 : 3 + wide + 2]
    result = convolve(up_lifted, w_last[:, :split]) + skip
    return jnp.transpose(result, (2, 0, 1))


def solution(mesh):
    placed = (P(None, "lat", "lon"), P(), P(), P(), P(), P(), P(), P(), P(), P(), P())
    return jax.shard_map(
        on_device, mesh=mesh, in_specs=placed, out_specs=P(None, "lat", "lon"), check_vma=False
    )
```
